256 devices in a mesh: ty: 16 (over z_hi, y), tx: 16 (over x, z_lo, core).
Axes of the slice: x: 4, y: 4, z: 8 (z_hi: 4, z_lo: 2; z = z_hi * 2 + z_lo), core: 2. Of those that a mesh axis runs over, the one named last changes fastest.
Arguments:
- object_slices: float32 [2, 2, 8192, 8192], P(None, None, 'ty', 'tx'), may hold values from -1.1 to 1.1
- probe: float32 [2, 256, 256], replicated, may hold values from -4.2 to 4.2
- fresnel_phase: float32 [256, 256], replicated, may hold values from -3.140625 to 3.140625
- intensity: float32 [16, 16, 4, 256, 256], P('ty', 'tx'), may hold values from 0.05 to 2
- offsets: int32 [16, 16, 4, 2], P('ty', 'tx'), may hold values from -128 to 384, as said below
- counts: int32 [16, 16], replicated, may hold values from 1 to 4, as said below
Outputs:
- new_object: float32 [2, 2, 8192, 8192], P(None, None, 'ty', 'tx')
The draws below stay inside these ranges and needn't reach their ends.
Inputs may be any that keep to these rules, and one draw needn't show every extreme that they name: The positions of a tile fill its slots 0 to counts - 1; some tile has 4. `offsets`: every window of 256 x 256 pixels lies inside the object.
All inputs are finite; a program needn't handle non-finite values.
Results may differ from the reference program's by a relative error of at most 0.0003.
Values sent between devices are 32-bit elements; how exact they have to be, the bound alone decides.
No kernel may reach another device: no remote copies, remote signals or barrier semaphores. Data moves between devices by JAX's collectives and lax.ppermute only.
A program may use at most 128 MiB of HBM per device.

```python
import math
import jax
import jax.numpy as jnp
from jax import lax

PATCH = 256
TILE = 512
SLICES = 2
CAP = 4
HALF = 128
GRID_Y = 16
GRID_X = 16
NPY = 8192
NPX = 8192


def draw_object_slices(key, part):
    key_amp, key_phase = jax.random.split(key)
    shape = (SLICES, NPY, NPX)
    amplitude = jax.random.uniform(key_amp, shape, jnp.float32, 0.6, 1.0)
    phase = jax.random.uniform(key_phase, shape, jnp.float32, -1.0, 1.0)
    return jnp.stack([amplitude * jnp.cos(phase), amplitude * jnp.sin(phase)], axis=1).astype(jnp.float32)


def draw_offsets(key, part):
    key_raw, key_y, key_x = jax.random.split(jax.random.fold_in(key, 11), 3)
    raw = jax.random.randint(key_raw, (GRID_Y, GRID_X, CAP, 2), -HALF, TILE - HALF + 1)
    tile_rows = jnp.arange(GRID_Y, dtype=jnp.int32)[:, None, None]
    tile_cols = jnp.arange(GRID_X, dtype=jnp.int32)[None, :, None]
    slot_index = jnp.arange(CAP, dtype=jnp.int32)[None, None, :]
    rows = jnp.clip(tile_rows * TILE + raw[..., 0], 0, GRID_Y * TILE - PATCH) - tile_rows * TILE
    cols = jnp.clip(tile_cols * TILE + raw[..., 1], 0, GRID_X * TILE - PATCH) - tile_cols * TILE
    pick_y = jax.random.randint(key_y, (), 1, GRID_Y - 1)
    pick_x = jax.random.randint(key_x, (), 1, GRID_X - 1)
    chosen = (tile_rows == pick_y) & (tile_cols == pick_x)
    rows = jnp.where(chosen & (slot_index == 0), -HALF, rows)
    rows = jnp.where(chosen & (slot_index == 1), TILE - HALF, rows)
    cols = jnp.where(chosen & (slot_index == 0), -HALF, cols)
    cols = jnp.where(chosen & (slot_index == 1), TILE - HALF, cols)
    return jnp.stack([rows, cols], axis=-1).astype(jnp.int32)


def draw_counts(key, part):
    key_base, key_y, key_x = jax.random.split(jax.random.fold_in(key, 23), 3)
    base = jax.random.randint(key_base, (GRID_Y, GRID_X), 1, 3)
    centre_y = jax.random.randint(key_y, (), 0, GRID_Y - 2)
    centre_x = jax.random.randint(key_x, (), 0, GRID_X // 2 - 1)
    rows = jnp.arange(GRID_Y, dtype=jnp.int32)[:, None]
    cols = jnp.arange(GRID_X, dtype=jnp.int32)[None, :]
    dense = (rows >= centre_y) & (rows <= centre_y + 2) & (cols >= centre_x) & (cols <= centre_x + 1)
    return jnp.where(dense, CAP, base).astype(jnp.int32)


def level_of(own_key, extent, pieces, low, largest):
    def one(position, parts):
        draws = jax.random.uniform(jax.random.fold_in(jax.random.fold_in(own_key, 6), position), (parts,), jnp.float32, low / len(pieces), largest / len(pieces))
        return jnp.repeat(jnp.exp(draws), extent[position] // parts).reshape((-1,) + (1,) * (len(extent) - position - 1))

    loudness = one(*pieces[0])
    for cut in pieces[1:]:
        loudness = loudness * one(*cut)
    return loudness


def centred(key, shape, width, bound, kind=jnp.bfloat16):
    result = jax.random.normal(key, shape, jnp.float32) * width
    return jnp.minimum(jnp.maximum(result, -bound), bound).astype(kind)


def setup_inputs(seed: int = 0) -> dict:
    splits = jax.random.split(jax.random.key(seed), 7)
    return {
        "object_slices": draw_object_slices(jax.random.fold_in(splits[6], 71), 0),
        "probe": centred(splits[1], (2, PATCH, PATCH), 0.7, 4.2, jnp.float32),
        "fresnel_phase": jnp.clip(jax.random.uniform(splits[2], (PATCH, PATCH), jnp.float32, -3.140625, 3.140625), -3.140625, 3.140625),
        "intensity": jnp.clip(jnp.exp(math.log(2.0) - 3.6888794 * jax.random.uniform(splits[3], (GRID_Y, GRID_X, CAP, PATCH, PATCH), jnp.float32) ** level_of(splits[3], (GRID_Y, GRID_X, CAP, PATCH, PATCH), ((0, 16), (1, 16)), -0.2, 0.2)), 0.05, 2.0),
        "offsets": draw_offsets(jax.random.fold_in(splits[6], 71), 0),
        "counts": draw_counts(jax.random.fold_in(splits[6], 71), 0),
    }


HIGH = lax.Precision.HIGHEST
STEP_SIZE = 0.25

def dft_basis(length):
    index = jnp.arange(length, dtype=jnp.int32)
    turns = index[:, None] * index[None, :] % length
    angles = turns.astype(jnp.float32) * (2.0 * math.pi / length)
    scale = 1.0 / math.sqrt(length)
    return (jnp.cos(angles) * scale, -jnp.sin(angles) * scale)

def matmul_high(left, right):
    return jnp.dot(left, right, precision=HIGH, preferred_element_type=jnp.float32)

def complex_matmul(left_re, left_im, right_re, right_im):
    real = matmul_high(left_re, right_re) - matmul_high(left_im, right_im)
    imag = matmul_high(left_re, right_im) + matmul_high(left_im, right_re)
    return (real, imag)

def forward_dft(field_re, field_im, basis_re, basis_im):
    temp_re, temp_im = complex_matmul(basis_re, basis_im, field_re, field_im)
    return complex_matmul(temp_re, temp_im, basis_re, basis_im)

def complex_times(left_re, left_im, right_re, right_im):
    return (left_re * right_re - left_im * right_im, left_re * right_im + left_im * right_re)

def conj_times(left_re, left_im, right_re, right_im):
    return (left_re * right_re + left_im * right_im, left_im * right_re - left_re * right_im)

def position_grad(window, measured, probe, kernel_re, kernel_im, basis_re, basis_im):
    first_re, first_im = complex_times(probe[0], probe[1], window[0, 0], window[0, 1])
    spec_re, spec_im = forward_dft(first_re, first_im, basis_re, basis_im)
    spec_re, spec_im = complex_times(kernel_re, kernel_im, spec_re, spec_im)
    phi_re, phi_im = forward_dft(spec_re, spec_im, basis_re, -basis_im)
    exit_re, exit_im = complex_times(phi_re, phi_im, window[1, 0], window[1, 1])
    far_re, far_im = forward_dft(exit_re, exit_im, basis_re, basis_im)
    misfit = far_re * far_re + far_im * far_im - measured
    back_re, back_im = forward_dft(misfit * far_re, misfit * far_im, basis_re, -basis_im)
    second_re, second_im = conj_times(back_re, back_im, phi_re, phi_im)
    wave_re, wave_im = conj_times(back_re, back_im, window[1, 0], window[1, 1])
    wave_re, wave_im = forward_dft(wave_re, wave_im, basis_re, basis_im)
    wave_re, wave_im = conj_times(wave_re, wave_im, kernel_re, kernel_im)
    wave_re, wave_im = forward_dft(wave_re, wave_im, basis_re, -basis_im)
    lead_re, lead_im = conj_times(wave_re, wave_im, probe[0], probe[1])
    return jnp.stack([jnp.stack([lead_re, lead_im]), jnp.stack([second_re, second_im])])

def reference(object_slices, probe, fresnel_phase, intensity, offsets, counts):
    basis_re, basis_im = dft_basis(PATCH)
    kernel_re = jnp.cos(fresnel_phase)
    kernel_im = jnp.sin(fresnel_phase)
    total = GRID_Y * GRID_X * CAP
    zero_index = jnp.zeros((), jnp.int32)

    def one_position(gradient, number):
        tile_y = number // (GRID_X * CAP)
        tile_x = number // CAP % GRID_X
        slot = number % CAP
        row = (tile_y * TILE + offsets[tile_y, tile_x, slot, 0]).astype(jnp.int32)
        column = (tile_x * TILE + offsets[tile_y, tile_x, slot, 1]).astype(jnp.int32)
        live = (slot < counts[tile_y, tile_x]).astype(jnp.float32)
        start = (zero_index, zero_index, row, column)
        window = lax.dynamic_slice(object_slices, start, (SLICES, 2, PATCH, PATCH))
        term = position_grad(window, intensity[tile_y, tile_x, slot], probe, kernel_re, kernel_im, basis_re, basis_im) * live
        current = lax.dynamic_slice(gradient, start, (SLICES, 2, PATCH, PATCH))
        return (lax.dynamic_update_slice(gradient, current + term, start), None)
    gradient, unused = lax.scan(one_position, jnp.zeros_like(object_slices), jnp.arange(total, dtype=jnp.int32))
    return object_slices - STEP_SIZE * gradient
```

```python
import math

import jax
import jax.numpy as jnp
from jax import lax
from jax.sharding import PartitionSpec as P

HIGH = lax.Precision.HIGHEST
FAST = lax.Precision.HIGH
STEP_SIZE = 0.25


def passed_along(value, axis, steps):
    count = lax.axis_size(axis)
    first, last = (max(0, -steps), min(count, count - steps))
    return lax.ppermute(value, axis, [(source, source + steps) for source in range(first, last)])


def extended(array, sides, width):
    for axis, dim in sides:
        size, length = (lax.axis_size(axis), array.shape[dim])
        up = [(i, (i + 1) % size) for i in range(size - 1)]
        down = [(j, i) for i, j in up]
        last = lax.slice_in_dim(array, length - width, length, axis=dim)
        first = lax.slice_in_dim(array, 0, width, axis=dim)
        before = lax.ppermute(last, axis, up)
        after = lax.ppermute(first, axis, down)
        array = jnp.concatenate([before, array, after], axis=dim)
    return array


def dft_basis(length):
    index = jnp.arange(length, dtype=jnp.int32)
    turns = index[:, None] * index[None, :] % length
    angles = turns.astype(jnp.float32) * (2.0 * math.pi / length)
    scale = 1.0 / math.sqrt(length)
    return (jnp.cos(angles) * scale, -jnp.sin(angles) * scale)


def matmul_high(left, right):
    return jnp.dot(left, right, precision=HIGH, preferred_element_type=jnp.float32)


def complex_matmul(left_re, left_im, right_re, right_im):
    real = matmul_high(left_re, right_re) - matmul_high(left_im, right_im)
    imag = matmul_high(left_re, right_im) + matmul_high(left_im, right_re)
    return (real, imag)


def forward_dft(field_re, field_im, basis_re, basis_im):
    temp_re, temp_im = complex_matmul(basis_re, basis_im, field_re, field_im)
    return complex_matmul(temp_re, temp_im, basis_re, basis_im)


def complex_times(left_re, left_im, right_re, right_im):
    return (left_re * right_re - left_im * right_im, left_re * right_im + left_im * right_re)


def conj_times(left_re, left_im, right_re, right_im):
    return (left_re * right_re + left_im * right_im, left_im * right_re - left_re * right_im)


def right_times(field_re, field_im, basis):
    count = field_re.shape[0]
    side = basis.shape[0]
    stacked = jnp.concatenate([field_re, field_im], axis=0)
    both = jnp.einsum("bjk,kl->bjl", stacked, basis, precision=FAST, preferred_element_type=jnp.float32)
    real = both[:count, :, :side] - both[count:, :, side:]
    imag = both[:count, :, side:] + both[count:, :, :side]
    return (real, imag)


def left_times(basis, field_re, field_im):
    side = basis.shape[1]
    stacked = jnp.concatenate([field_re, field_im], axis=2)
    both = jnp.einsum("ij,bjl->bil", basis, stacked, precision=FAST, preferred_element_type=jnp.float32)
    real = both[:, :side, :side] - both[:, side:, side:]
    imag = both[:, :side, side:] + both[:, side:, :side]
    return (real, imag)


def two_sided(field_re, field_im, bases):
    left, right = bases
    temp_re, temp_im = left_times(left, field_re, field_im)
    return right_times(temp_re, temp_im, right)


def batched_grad(window, measured, probe, kernel_re, kernel_im, plain, conjugate):
    first_re, first_im = complex_times(probe[0], probe[1], window[:, 0, 0], window[:, 0, 1])
    spec_re, spec_im = two_sided(first_re, first_im, plain)
    spec_re, spec_im = complex_times(kernel_re, kernel_im, spec_re, spec_im)
    phi_re, phi_im = two_sided(spec_re, spec_im, conjugate)
    exit_re, exit_im = complex_times(phi_re, phi_im, window[:, 1, 0], window[:, 1, 1])
    far_re, far_im = two_sided(exit_re, exit_im, plain)
    misfit = far_re * far_re + far_im * far_im - measured
    back_re, back_im = two_sided(misfit * far_re, misfit * far_im, conjugate)
    second_re, second_im = conj_times(back_re, back_im, phi_re, phi_im)
    wave_re, wave_im = conj_times(back_re, back_im, window[:, 1, 0], window[:, 1, 1])
    wave_re, wave_im = two_sided(wave_re, wave_im, plain)
    wave_re, wave_im = conj_times(wave_re, wave_im, kernel_re, kernel_im)
    wave_re, wave_im = two_sided(wave_re, wave_im, conjugate)
    lead_re, lead_im = conj_times(wave_re, wave_im, probe[0], probe[1])
    return jnp.stack([jnp.stack([lead_re, lead_im], 1), jnp.stack([second_re, second_im], 1)], 1)


def from_column(piece, steps):
    return passed_along(piece, "tx", steps)


def from_row(piece, steps):
    return passed_along(piece, "ty", steps)


def shards(object_slices, probe, fresnel_phase, intensity, offsets, counts):
    patch = probe.shape[-1]
    half = patch // 2
    tile = object_slices.shape[-1]
    layers = object_slices.shape[0]
    basis_re, basis_im = dft_basis(patch)
    kernel_re = jnp.cos(fresnel_phase)
    kernel_im = jnp.sin(fresnel_phase)
    measured = intensity[0, 0]
    places = offsets[0, 0] + half
    window_shape = (layers, 2, patch, patch)
    zero_index = jnp.zeros((), jnp.int32)
    padded = extended(object_slices, (("ty", 2), ("tx", 3)), half)
    row_here = lax.axis_index("ty")
    col_here = lax.axis_index("tx")
    mine = counts[row_here, col_here]

    def start_of(slot):
        return (zero_index, zero_index, places[slot, 0], places[slot, 1])

    def window_at(slot):
        return lax.dynamic_slice(padded, start_of(slot), window_shape)

    plain = (
        jnp.concatenate([basis_re, basis_im], axis=0),
        jnp.concatenate([basis_re, basis_im], axis=1),
    )
    conjugate = (
        jnp.concatenate([basis_re, -basis_im], axis=0),
        jnp.concatenate([basis_re, -basis_im], axis=1),
    )
    slots = measured.shape[0]
    windows = jnp.stack([window_at(slot) for slot in range(slots)])
    terms = batched_grad(windows, measured, probe, kernel_re, kernel_im, plain, conjugate)

    def add_at(gradient, slot, term):
        start = start_of(slot)
        current = lax.dynamic_slice(gradient, start, window_shape)
        term = jnp.where(slot < mine, term, jnp.zeros_like(term))
        return lax.dynamic_update_slice(gradient, current + term, start)

    gradient = jnp.zeros((layers, 2, tile + 2 * half, tile + 2 * half), jnp.float32)
    for slot in range(slots):
        gradient = add_at(gradient, slot, terms[slot])
    core_cols = gradient[:, :, :, half : half + tile]
    core_cols = core_cols.at[:, :, :, :half].add(from_column(gradient[:, :, :, half + tile :], 1))
    core_cols = core_cols.at[:, :, :, tile - half :].add(from_column(gradient[:, :, :, :half], -1))
    core = core_cols[:, :, half : half + tile]
    core = core.at[:, :, :half].add(from_row(core_cols[:, :, half + tile :], 1))
    core = core.at[:, :, tile - half :].add(from_row(core_cols[:, :, :half], -1))
    return object_slices - STEP_SIZE * core


def solution(mesh):
    placed = (
        P(None, None, "ty", "tx"),
        P(),
        P(),
        P("ty", "tx", None, None, None),
        P("ty", "tx", None, None),
        P(),
    )
    return jax.shard_map(
        shards, mesh=mesh, in_specs=placed, out_specs=P(None, None, "ty", "tx"), check_vma=False
    )
```

```python
import math

import jax
import jax.numpy as jnp
from jax import lax
from jax.sharding import PartitionSpec as P

HIGH = lax.Precision.HIGHEST
FAST = lax.Precision.HIGH
STEP_SIZE = 0.25


def dft_basis(length):
    index = jnp.arange(length, dtype=jnp.int32)
    turns = index[:, None] * index[None, :] % length
    angles = turns.astype(jnp.float32) * (2.0 * math.pi / length)
    scale = 1.0 / math.sqrt(length)
    return (jnp.cos(angles) * scale, -jnp.sin(angles) * scale)


def matmul_high(left, right):
    return jnp.dot(left, right, precision=HIGH, preferred_element_type=jnp.float32)


def complex_matmul(left_re, left_im, right_re, right_im):
    real = matmul_high(left_re, right_re) - matmul_high(left_im, right_im)
    imag = matmul_high(left_re, right_im) + matmul_high(left_im, right_re)
    return (real, imag)


def forward_dft(field_re, field_im, basis_re, basis_im):
    temp_re, temp_im = complex_matmul(basis_re, basis_im, field_re, field_im)
    return complex_matmul(temp_re, temp_im, basis_re, basis_im)


def complex_times(left_re, left_im, right_re, right_im):
    return (left_re * right_re - left_im * right_im, left_re * right_im + left_im * right_re)


def conj_times(left_re, left_im, right_re, right_im):
    return (left_re * right_re + left_im * right_im, left_im * right_re - left_re * right_im)


def right_times(field_re, field_im, basis):
    count = field_re.shape[0]
    side = basis.shape[0]
    stacked = jnp.concatenate([field_re, field_im], axis=0)
    both = jnp.einsum("bjk,kl->bjl", stacked, basis, precision=FAST, preferred_element_type=jnp.float32)
    real = both[:count, :, :side] - both[count:, :, side:]
    imag = both[:count, :, side:] + both[count:, :, :side]
    return (real, imag)


def left_times(basis, field_re, field_im):
    side = basis.shape[1]
    stacked = jnp.concatenate([field_re, field_im], axis=2)
    both = jnp.einsum("ij,bjl->bil", basis, stacked, precision=FAST, preferred_element_type=jnp.float32)
    real = both[:, :side, :side] - both[:, side:, side:]
    imag = both[:, :side, side:] + both[:, side:, :side]
    return (real, imag)


def two_sided(field_re, field_im, bases):
    left, right = bases
    temp_re, temp_im = left_times(left, field_re, field_im)
    return right_times(temp_re, temp_im, right)


def batched_grad(window, measured, probe, kernel_re, kernel_im, plain, conjugate):
    first_re, first_im = complex_times(probe[0], probe[1], window[:, 0, 0], window[:, 0, 1])
    spec_re, spec_im = two_sided(first_re, first_im, plain)
    spec_re, spec_im = complex_times(kernel_re, kernel_im, spec_re, spec_im)
    phi_re, phi_im = two_sided(spec_re, spec_im, conjugate)
    exit_re, exit_im = complex_times(phi_re, phi_im, window[:, 1, 0], window[:, 1, 1])
    far_re, far_im = two_sided(exit_re, exit_im, plain)
    misfit = far_re * far_re + far_im * far_im - measured
    back_re, back_im = two_sided(misfit * far_re, misfit * far_im, conjugate)
    second_re, second_im = conj_times(back_re, back_im, phi_re, phi_im)
    wave_re, wave_im = conj_times(back_re, back_im, window[:, 1, 0], window[:, 1, 1])
    wave_re, wave_im = two_sided(wave_re, wave_im, plain)
    wave_re, wave_im = conj_times(wave_re, wave_im, kernel_re, kernel_im)
    wave_re, wave_im = two_sided(wave_re, wave_im, conjugate)
    lead_re, lead_im = conj_times(wave_re, wave_im, probe[0], probe[1])
    return jnp.stack([jnp.stack([lead_re, lead_im], 1), jnp.stack([second_re, second_im], 1)], 1)


def neighbour_pairs(rows, cols, down, right):
    pairs = []
    for row in range(rows):
        for col in range(cols):
            to_row, to_col = (row + down, col + right)
            if 0 <= to_row < rows and 0 <= to_col < cols:
                pairs.append((row * cols + col, to_row * cols + to_col))
    return pairs


def from_neighbour(piece, down, right):
    rows, cols = (lax.axis_size("ty"), lax.axis_size("tx"))
    return lax.ppermute(piece, ("ty", "tx"), neighbour_pairs(rows, cols, down, right))


def with_halo(tile_data, half):
    size = tile_data.shape[-1]
    low, high = (slice(0, half), slice(size - half, size))
    every = slice(None)

    def got(down, right):
        rows = {1: high, 0: every, -1: low}[down]
        cols = {1: high, 0: every, -1: low}[right]
        return from_neighbour(tile_data[:, :, rows, cols], down, right)

    band = lambda down: jnp.concatenate([got(down, 1), got(down, 0), got(down, -1)], axis=3)
    middle = jnp.concatenate([got(0, 1), tile_data, got(0, -1)], axis=3)
    return jnp.concatenate([band(1), middle, band(-1)], axis=2)


def fold_halo(canvas, half):
    size = canvas.shape[-1] - 2 * half
    parts = {1: slice(half + size, 2 * half + size), 0: slice(half, half + size), -1: slice(0, half)}
    places = {1: slice(0, half), 0: slice(0, size), -1: slice(size - half, size)}
    core = canvas[:, :, half : half + size, half : half + size]
    for down in (1, 0, -1):
        for right in (1, 0, -1):
            if down == 0 and right == 0:
                continue
            piece = from_neighbour(canvas[:, :, parts[down], parts[right]], down, right)
            core = core.at[:, :, places[down], places[right]].add(piece)
    return core


def shards(object_slices, probe, fresnel_phase, intensity, offsets, counts):
    patch = probe.shape[-1]
    half = patch // 2
    tile = object_slices.shape[-1]
    layers = object_slices.shape[0]
    basis_re, basis_im = dft_basis(patch)
    kernel_re = jnp.cos(fresnel_phase)
    kernel_im = jnp.sin(fresnel_phase)
    measured = intensity[0, 0]
    places = offsets[0, 0] + half
    window_shape = (layers, 2, patch, patch)
    zero_index = jnp.zeros((), jnp.int32)
    padded = with_halo(object_slices, half)
    row_here = lax.axis_index("ty")
    col_here = lax.axis_index("tx")
    mine = counts[row_here, col_here]

    def start_of(slot):
        return (zero_index, zero_index, places[slot, 0], places[slot, 1])

    def window_at(slot):
        return lax.dynamic_slice(padded, start_of(slot), window_shape)

    plain = (
        jnp.concatenate([basis_re, basis_im], axis=0),
        jnp.concatenate([basis_re, basis_im], axis=1),
    )
    conjugate = (
        jnp.concatenate([basis_re, -basis_im], axis=0),
        jnp.concatenate([basis_re, -basis_im], axis=1),
    )
    slots = measured.shape[0]
    windows = jnp.stack([window_at(slot) for slot in range(slots)])
    terms = batched_grad(windows, measured, probe, kernel_re, kernel_im, plain, conjugate)
    span = tile + 2 * half
    block = patch + half
    last_block = (span - block) // half

    def add_at(gradient, slot, term):
        row, col = (places[slot, 0], places[slot, 1])
        block_row = jnp.minimum(row // half, last_block)
        block_col = jnp.minimum(col // half, last_block)
        term = jnp.where(slot < mine, term, jnp.zeros_like(term))
        spread = jnp.pad(term, ((0, 0), (0, 0), (half, half), (half, half)))
        inner = (zero_index, zero_index, half - (row - block_row * half), half - (col - block_col * half))
        shifted = lax.dynamic_slice(spread, inner, (layers, 2, block, block))
        start = (zero_index, zero_index, block_row * half, block_col * half)
        current = lax.dynamic_slice(gradient, start, shifted.shape)
        return lax.dynamic_update_slice(gradient, current + shifted, start)

    gradient = jnp.zeros((layers, 2, span, span), jnp.float32)
    for slot in range(slots):
        gradient = add_at(gradient, slot, terms[slot])
    core = fold_halo(gradient, half)
    return object_slices - STEP_SIZE * core


def solution(mesh):
    placed = (
        P(None, None, "ty", "tx"),
        P(),
        P(),
        P("ty", "tx", None, None, None),
        P("ty", "tx", None, None),
        P(),
    )
    return jax.shard_map(
        shards, mesh=mesh, in_specs=placed, out_specs=P(None, None, "ty", "tx"), check_vma=False
    )
```

```python
import math

import jax
import jax.numpy as jnp
from jax import lax
from jax.sharding import PartitionSpec as P

HIGH = lax.Precision.HIGHEST
FAST = lax.Precision.HIGH
STEP_SIZE = 0.25
ROW_GROUP = 4
DIRECT_COLS = 128


def dft_basis(length):
    index = jnp.arange(length, dtype=jnp.int32)
    turns = index[:, None] * index[None, :] % length
    angles = turns.astype(jnp.float32) * (2.0 * math.pi / length)
    scale = 1.0 / math.sqrt(length)
    return (jnp.cos(angles) * scale, -jnp.sin(angles) * scale)


def matmul_high(left, right):
    return jnp.dot(left, right, precision=HIGH, preferred_element_type=jnp.float32)


def complex_matmul(left_re, left_im, right_re, right_im):
    real = matmul_high(left_re, right_re) - matmul_high(left_im, right_im)
    imag = matmul_high(left_re, right_im) + matmul_high(left_im, right_re)
    return (real, imag)


def forward_dft(field_re, field_im, basis_re, basis_im):
    temp_re, temp_im = complex_matmul(basis_re, basis_im, field_re, field_im)
    return complex_matmul(temp_re, temp_im, basis_re, basis_im)


def complex_times(left_re, left_im, right_re, right_im):
    return (left_re * right_re - left_im * right_im, left_re * right_im + left_im * right_re)


def conj_times(left_re, left_im, right_re, right_im):
    return (left_re * right_re + left_im * right_im, left_im * right_re - left_re * right_im)


def right_times(field_re, field_im, basis):
    count = field_re.shape[0]
    side = basis.shape[0]
    stacked = jnp.concatenate([field_re, field_im], axis=0)
    both = jnp.einsum("bjk,kl->bjl", stacked, basis, precision=FAST, preferred_element_type=jnp.float32)
    real = both[:count, :, :side] - both[count:, :, side:]
    imag = both[:count, :, side:] + both[count:, :, :side]
    return (real, imag)


def left_times(basis, field_re, field_im):
    side = basis.shape[1]
    stacked = jnp.concatenate([field_re, field_im], axis=2)
    both = jnp.einsum("ij,bjl->bil", basis, stacked, precision=FAST, preferred_element_type=jnp.float32)
    real = both[:, :side, :side] - both[:, side:, side:]
    imag = both[:, :side, side:] + both[:, side:, :side]
    return (real, imag)


def two_sided(field_re, field_im, bases):
    left, right = bases
    temp_re, temp_im = left_times(left, field_re, field_im)
    return right_times(temp_re, temp_im, right)


def batched_grad(window, measured, probe, kernel_re, kernel_im, plain, conjugate):
    first_re, first_im = complex_times(probe[0], probe[1], window[:, 0, 0], window[:, 0, 1])
    spec_re, spec_im = two_sided(first_re, first_im, plain)
    spec_re, spec_im = complex_times(kernel_re, kernel_im, spec_re, spec_im)
    phi_re, phi_im = two_sided(spec_re, spec_im, conjugate)
    exit_re, exit_im = complex_times(phi_re, phi_im, window[:, 1, 0], window[:, 1, 1])
    far_re, far_im = two_sided(exit_re, exit_im, plain)
    misfit = far_re * far_re + far_im * far_im - measured
    back_re, back_im = two_sided(misfit * far_re, misfit * far_im, conjugate)
    second_re, second_im = conj_times(back_re, back_im, phi_re, phi_im)
    wave_re, wave_im = conj_times(back_re, back_im, window[:, 1, 0], window[:, 1, 1])
    wave_re, wave_im = two_sided(wave_re, wave_im, plain)
    wave_re, wave_im = conj_times(wave_re, wave_im, kernel_re, kernel_im)
    wave_re, wave_im = two_sided(wave_re, wave_im, conjugate)
    lead_re, lead_im = conj_times(wave_re, wave_im, probe[0], probe[1])
    return jnp.stack([jnp.stack([lead_re, lead_im], 1), jnp.stack([second_re, second_im], 1)], 1)


def neighbour_pairs(rows, cols, down, right):
    pairs = []
    for row in range(rows):
        for col in range(cols):
            to_row, to_col = (row + down, col + right)
            if 0 <= to_row < rows and 0 <= to_col < cols:
                pairs.append((row * cols + col, to_row * cols + to_col))
    return pairs


def row_pairs(rows, step, keep):
    return [(row, row + step) for row in range(rows) if 0 <= row + step < rows and keep(row)]


def along_rows(piece, step):
    rows = lax.axis_size("ty")
    group = ROW_GROUP
    edge = group - 1 if step > 0 else 0
    direct_part, detour_part = (piece[..., :DIRECT_COLS], piece[..., DIRECT_COLS:])
    direct = lax.ppermute(direct_part, "ty", row_pairs(rows, step, lambda row: True))
    inside = row_pairs(rows, step, lambda row: row % group != edge)
    turned = [(row, row - step * (group - 1)) for row, _ in row_pairs(rows, step, lambda row: row % group == edge)]
    first = lax.ppermute(detour_part, "ty", inside + turned)
    carried = [(row, row + step * group) for _, row in turned]
    second = lax.ppermute(first, "ty", carried)
    landing = lax.axis_index("ty") % group == group - 1 - edge
    detour = jnp.where(landing, second, first)
    return jnp.concatenate([direct, detour], axis=-1)


def from_neighbour(piece, down, right):
    rows, cols = (lax.axis_size("ty"), lax.axis_size("tx"))
    if right == 0:
        return along_rows(piece, down)
    return lax.ppermute(piece, ("ty", "tx"), neighbour_pairs(rows, cols, down, right))


def with_halo(tile_data, half):
    size = tile_data.shape[-1]
    low, high = (slice(0, half), slice(size - half, size))
    every = slice(None)

    def got(down, right):
        rows = {1: high, 0: every, -1: low}[down]
        cols = {1: high, 0: every, -1: low}[right]
        return from_neighbour(tile_data[:, :, rows, cols], down, right)

    band = lambda down: jnp.concatenate([got(down, 1), got(down, 0), got(down, -1)], axis=3)
    middle = jnp.concatenate([got(0, 1), tile_data, got(0, -1)], axis=3)
    return jnp.concatenate([band(1), middle, band(-1)], axis=2)


def fold_halo(canvas, half):
    size = canvas.shape[-1] - 2 * half
    parts = {1: slice(half + size, 2 * half + size), 0: slice(half, half + size), -1: slice(0, half)}
    places = {1: slice(0, half), 0: slice(0, size), -1: slice(size - half, size)}
    core = canvas[:, :, half : half + size, half : half + size]
    for down in (1, 0, -1):
        for right in (1, 0, -1):
            if down == 0 and right == 0:
                continue
            piece = from_neighbour(canvas[:, :, parts[down], parts[right]], down, right)
            core = core.at[:, :, places[down], places[right]].add(piece)
    return core


def shards(object_slices, probe, fresnel_phase, intensity, offsets, counts):
    patch = probe.shape[-1]
    half = patch // 2
    tile = object_slices.shape[-1]
    layers = object_slices.shape[0]
    basis_re, basis_im = dft_basis(patch)
    kernel_re = jnp.cos(fresnel_phase)
    kernel_im = jnp.sin(fresnel_phase)
    measured = intensity[0, 0]
    places = offsets[0, 0] + half
    window_shape = (layers, 2, patch, patch)
    zero_index = jnp.zeros((), jnp.int32)
    padded = with_halo(object_slices, half)
    row_here = lax.axis_index("ty")
    col_here = lax.axis_index("tx")
    mine = counts[row_here, col_here]

    def start_of(slot):
        return (zero_index, zero_index, places[slot, 0], places[slot, 1])

    def window_at(slot):
        return lax.dynamic_slice(padded, start_of(slot), window_shape)

    plain = (
        jnp.concatenate([basis_re, basis_im], axis=0),
        jnp.concatenate([basis_re, basis_im], axis=1),
    )
    conjugate = (
        jnp.concatenate([basis_re, -basis_im], axis=0),
        jnp.concatenate([basis_re, -basis_im], axis=1),
    )
    slots = measured.shape[0]
    windows = jnp.stack([window_at(slot) for slot in range(slots)])
    terms = batched_grad(windows, measured, probe, kernel_re, kernel_im, plain, conjugate)
    span = tile + 2 * half
    block = patch + half
    last_block = (span - block) // half

    def add_at(gradient, slot, term):
        row, col = (places[slot, 0], places[slot, 1])
        block_row = jnp.minimum(row // half, last_block)
        block_col = jnp.minimum(col // half, last_block)
        term = jnp.where(slot < mine, term, jnp.zeros_like(term))
        spread = jnp.pad(term, ((0, 0), (0, 0), (half, half), (half, half)))
        inner = (zero_index, zero_index, half - (row - block_row * half), half - (col - block_col * half))
        shifted = lax.dynamic_slice(spread, inner, (layers, 2, block, block))
        start = (zero_index, zero_index, block_row * half, block_col * half)
        current = lax.dynamic_slice(gradient, start, shifted.shape)
        return lax.dynamic_update_slice(gradient, current + shifted, start)

    gradient = jnp.zeros((layers, 2, span, span), jnp.float32)
    for slot in range(slots):
        gradient = add_at(gradient, slot, terms[slot])
    core = fold_halo(gradient, half)
    return object_slices - STEP_SIZE * core


def solution(mesh):
    placed = (
        P(None, None, "ty", "tx"),
        P(),
        P(),
        P("ty", "tx", None, None, None),
        P("ty", "tx", None, None),
        P(),
    )
    return jax.shard_map(
        shards, mesh=mesh, in_specs=placed, out_specs=P(None, None, "ty", "tx"), check_vma=False
    )
```

```python
import math

import jax
import jax.numpy as jnp
from jax import lax
from jax.sharding import PartitionSpec as P

HIGH = lax.Precision.HIGHEST
FAST = lax.Precision.HIGH
STEP_SIZE = 0.25


def dft_basis(length):
    index = jnp.arange(length, dtype=jnp.int32)
    turns = index[:, None] * index[None, :] % length
    angles = turns.astype(jnp.float32) * (2.0 * math.pi / length)
    scale = 1.0 / math.sqrt(length)
    return (jnp.cos(angles) * scale, -jnp.sin(angles) * scale)


def matmul_high(left, right):
    return jnp.dot(left, right, precision=HIGH, preferred_element_type=jnp.float32)


def complex_matmul(left_re, left_im, right_re, right_im):
    real = matmul_high(left_re, right_re) - matmul_high(left_im, right_im)
    imag = matmul_high(left_re, right_im) + matmul_high(left_im, right_re)
    return (real, imag)


def forward_dft(field_re, field_im, basis_re, basis_im):
    temp_re, temp_im = complex_matmul(basis_re, basis_im, field_re, field_im)
    return complex_matmul(temp_re, temp_im, basis_re, basis_im)


def complex_times(left_re, left_im, right_re, right_im):
    return (left_re * right_re - left_im * right_im, left_re * right_im + left_im * right_re)


def conj_times(left_re, left_im, right_re, right_im):
    return (left_re * right_re + left_im * right_im, left_im * right_re - left_re * right_im)


def right_times(field_re, field_im, basis):
    count = field_re.shape[0]
    side = basis.shape[0]
    stacked = jnp.concatenate([field_re, field_im], axis=0)
    both = jnp.einsum("bjk,kl->bjl", stacked, basis, precision=FAST, preferred_element_type=jnp.float32)
    real = both[:count, :, :side] - both[count:, :, side:]
    imag = both[:count, :, side:] + both[count:, :, :side]
    return (real, imag)


def left_times(basis, field_re, field_im):
    side = basis.shape[1]
    stacked = jnp.concatenate([field_re, field_im], axis=2)
    both = jnp.einsum("ij,bjl->bil", basis, stacked, precision=FAST, preferred_element_type=jnp.float32)
    real = both[:, :side, :side] - both[:, side:, side:]
    imag = both[:, :side, side:] + both[:, side:, :side]
    return (real, imag)


def two_sided(field_re, field_im, bases):
    left, right = bases
    temp_re, temp_im = left_times(left, field_re, field_im)
    return right_times(temp_re, temp_im, right)


def batched_grad(window, measured, probe, kernel_re, kernel_im, plain, conjugate):
    first_re, first_im = complex_times(probe[0], probe[1], window[:, 0, 0], window[:, 0, 1])
    spec_re, spec_im = two_sided(first_re, first_im, plain)
    spec_re, spec_im = complex_times(kernel_re, kernel_im, spec_re, spec_im)
    phi_re, phi_im = two_sided(spec_re, spec_im, conjugate)
    exit_re, exit_im = complex_times(phi_re, phi_im, window[:, 1, 0], window[:, 1, 1])
    far_re, far_im = two_sided(exit_re, exit_im, plain)
    misfit = far_re * far_re + far_im * far_im - measured
    back_re, back_im = two_sided(misfit * far_re, misfit * far_im, conjugate)
    second_re, second_im = conj_times(back_re, back_im, phi_re, phi_im)
    wave_re, wave_im = conj_times(back_re, back_im, window[:, 1, 0], window[:, 1, 1])
    wave_re, wave_im = two_sided(wave_re, wave_im, plain)
    wave_re, wave_im = conj_times(wave_re, wave_im, kernel_re, kernel_im)
    wave_re, wave_im = two_sided(wave_re, wave_im, conjugate)
    lead_re, lead_im = conj_times(wave_re, wave_im, probe[0], probe[1])
    return jnp.stack([jnp.stack([lead_re, lead_im], 1), jnp.stack([second_re, second_im], 1)], 1)


def neighbour_pairs(rows, cols, down, right):
    pairs = []
    for row in range(rows):
        for col in range(cols):
            to_row, to_col = (row + down, col + right)
            if 0 <= to_row < rows and 0 <= to_col < cols:
                pairs.append((row * cols + col, to_row * cols + to_col))
    return pairs


def from_neighbour(piece, down, right):
    rows, cols = (lax.axis_size("ty"), lax.axis_size("tx"))
    return lax.ppermute(piece, ("ty", "tx"), neighbour_pairs(rows, cols, down, right))


def with_halo(tile_data, half):
    size = tile_data.shape[-1]
    low, high = (slice(0, half), slice(size - half, size))
    every = slice(None)

    def got(down, right):
        rows = {1: high, 0: every, -1: low}[down]
        cols = {1: high, 0: every, -1: low}[right]
        return from_neighbour(tile_data[:, :, rows, cols], down, right)

    band = lambda down: jnp.concatenate([got(down, 1), got(down, 0), got(down, -1)], axis=3)
    middle = jnp.concatenate([got(0, 1), tile_data, got(0, -1)], axis=3)
    return jnp.concatenate([band(1), middle, band(-1)], axis=2)


def fold_halo(canvas, half):
    size = canvas.shape[-1] - 2 * half
    parts = {1: slice(half + size, 2 * half + size), 0: slice(half, half + size), -1: slice(0, half)}
    places = {1: slice(0, half), 0: slice(0, size), -1: slice(size - half, size)}
    core = canvas[:, :, half : half + size, half : half + size]
    for down in (1, 0, -1):
        for right in (1, 0, -1):
            if down == 0 and right == 0:
                continue
            piece = from_neighbour(canvas[:, :, parts[down], parts[right]], down, right)
            spots = [places[down], places[right]]
            widths = [(spot.start, size - spot.stop) for spot in spots]
            core = core + jnp.pad(piece, [(0, 0), (0, 0)] + widths)
    return core


def shards(object_slices, probe, fresnel_phase, intensity, offsets, counts):
    patch = probe.shape[-1]
    half = patch // 2
    tile = object_slices.shape[-1]
    layers = object_slices.shape[0]
    basis_re, basis_im = dft_basis(patch)
    kernel_re = jnp.cos(fresnel_phase)
    kernel_im = jnp.sin(fresnel_phase)
    measured = intensity[0, 0]
    places = offsets[0, 0] + half
    window_shape = (layers, 2, patch, patch)
    zero_index = jnp.zeros((), jnp.int32)
    padded = with_halo(object_slices, half)
    row_here = lax.axis_index("ty")
    col_here = lax.axis_index("tx")
    mine = counts[row_here, col_here]

    def start_of(slot):
        return (zero_index, zero_index, places[slot, 0], places[slot, 1])

    def window_at(slot):
        return lax.dynamic_slice(padded, start_of(slot), window_shape)

    plain = (
        jnp.concatenate([basis_re, basis_im], axis=0),
        jnp.concatenate([basis_re, basis_im], axis=1),
    )
    conjugate = (
        jnp.concatenate([basis_re, -basis_im], axis=0),
        jnp.concatenate([basis_re, -basis_im], axis=1),
    )
    slots = measured.shape[0]
    windows = jnp.stack([window_at(slot) for slot in range(slots)])
    terms = batched_grad(windows, measured, probe, kernel_re, kernel_im, plain, conjugate)
    span = tile + 2 * half
    block = patch + half
    last_block = (span - block) // half

    def add_at(gradient, slot, term):
        row, col = (places[slot, 0], places[slot, 1])
        block_row = jnp.minimum(row // half, last_block)
        block_col = jnp.minimum(col // half, last_block)
        term = jnp.where(slot < mine, term, jnp.zeros_like(term))
        spread = jnp.pad(term, ((0, 0), (0, 0), (half, half), (half, half)))
        inner = (zero_index, zero_index, half - (row - block_row * half), half - (col - block_col * half))
        shifted = lax.dynamic_slice(spread, inner, (layers, 2, block, block))
        start = (zero_index, zero_index, block_row * half, block_col * half)
        current = lax.dynamic_slice(gradient, start, shifted.shape)
        return lax.dynamic_update_slice(gradient, current + shifted, start)

    gradient = jnp.zeros((layers, 2, span, span), jnp.float32)
    for slot in range(slots):
        gradient = add_at(gradient, slot, terms[slot])
    core = fold_halo(gradient, half)
    return object_slices - STEP_SIZE * core


def solution(mesh):
    placed = (
        P(None, None, "ty", "tx"),
        P(),
        P(),
        P("ty", "tx", None, None, None),
        P("ty", "tx", None, None),
        P(),
    )
    return jax.shard_map(
        shards, mesh=mesh, in_specs=placed, out_specs=P(None, None, "ty", "tx"), check_vma=False
    )
```

```python
import math

import jax
import jax.numpy as jnp
from jax import lax
from jax.sharding import PartitionSpec as P

HIGH = lax.Precision.HIGHEST
FAST = lax.Precision.HIGH
STEP_SIZE = 0.25


def dft_basis(length):
    index = jnp.arange(length, dtype=jnp.int32)
    turns = index[:, None] * index[None, :] % length
    angles = turns.astype(jnp.float32) * (2.0 * math.pi / length)
    scale = 1.0 / math.sqrt(length)
    return (jnp.cos(angles) * scale, -jnp.sin(angles) * scale)


def matmul_high(left, right):
    return jnp.dot(left, right, precision=HIGH, preferred_element_type=jnp.float32)


def complex_matmul(left_re, left_im, right_re, right_im):
    real = matmul_high(left_re, right_re) - matmul_high(left_im, right_im)
    imag = matmul_high(left_re, right_im) + matmul_high(left_im, right_re)
    return (real, imag)


def forward_dft(field_re, field_im, basis_re, basis_im):
    temp_re, temp_im = complex_matmul(basis_re, basis_im, field_re, field_im)
    return complex_matmul(temp_re, temp_im, basis_re, basis_im)


def complex_times(left_re, left_im, right_re, right_im):
    return (left_re * right_re - left_im * right_im, left_re * right_im + left_im * right_re)


def conj_times(left_re, left_im, right_re, right_im):
    return (left_re * right_re + left_im * right_im, left_im * right_re - left_re * right_im)


def matmul_fast(left, right):
    return jnp.dot(left, right, precision=FAST, preferred_element_type=jnp.float32)


def right_times(field_re, field_im, basis):
    count = field_re.shape[0]
    side = basis.shape[0]
    stacked = jnp.concatenate([field_re, field_im], axis=0)
    both = jnp.einsum("bjk,kl->bjl", stacked, basis, precision=FAST, preferred_element_type=jnp.float32)
    real = both[:count, :, :side] - both[count:, :, side:]
    imag = both[:count, :, side:] + both[count:, :, :side]
    return (real, imag)


def left_times(basis, field_re, field_im):
    side = basis.shape[1]
    stacked = jnp.concatenate([field_re, field_im], axis=2)
    both = jnp.stack([matmul_fast(basis, one) for one in stacked])
    real = both[:, :side, :side] - both[:, side:, side:]
    imag = both[:, :side, side:] + both[:, side:, :side]
    return (real, imag)


def two_sided(field_re, field_im, bases):
    left, right = bases
    temp_re, temp_im = left_times(left, field_re, field_im)
    return right_times(temp_re, temp_im, right)


def batched_grad(window, measured, probe, kernel_re, kernel_im, plain, conjugate):
    first_re, first_im = complex_times(probe[0], probe[1], window[:, 0, 0], window[:, 0, 1])
    spec_re, spec_im = two_sided(first_re, first_im, plain)
    spec_re, spec_im = complex_times(kernel_re, kernel_im, spec_re, spec_im)
    phi_re, phi_im = two_sided(spec_re, spec_im, conjugate)
    exit_re, exit_im = complex_times(phi_re, phi_im, window[:, 1, 0], window[:, 1, 1])
    far_re, far_im = two_sided(exit_re, exit_im, plain)
    misfit = far_re * far_re + far_im * far_im - measured
    back_re, back_im = two_sided(misfit * far_re, misfit * far_im, conjugate)
    second_re, second_im = conj_times(back_re, back_im, phi_re, phi_im)
    wave_re, wave_im = conj_times(back_re, back_im, window[:, 1, 0], window[:, 1, 1])
    wave_re, wave_im = two_sided(wave_re, wave_im, plain)
    wave_re, wave_im = conj_times(wave_re, wave_im, kernel_re, kernel_im)
    wave_re, wave_im = two_sided(wave_re, wave_im, conjugate)
    lead_re, lead_im = conj_times(wave_re, wave_im, probe[0], probe[1])
    return jnp.stack([jnp.stack([lead_re, lead_im], 1), jnp.stack([second_re, second_im], 1)], 1)


def neighbour_pairs(rows, cols, down, right):
    pairs = []
    for row in range(rows):
        for col in range(cols):
            to_row, to_col = (row + down, col + right)
            if 0 <= to_row < rows and 0 <= to_col < cols:
                pairs.append((row * cols + col, to_row * cols + to_col))
    return pairs


def from_neighbour(piece, down, right):
    rows, cols = (lax.axis_size("ty"), lax.axis_size("tx"))
    return lax.ppermute(piece, ("ty", "tx"), neighbour_pairs(rows, cols, down, right))


def with_halo(tile_data, half):
    size = tile_data.shape[-1]
    low, high = (slice(0, half), slice(size - half, size))
    every = slice(None)

    def got(down, right):
        rows = {1: high, 0: every, -1: low}[down]
        cols = {1: high, 0: every, -1: low}[right]
        return from_neighbour(tile_data[:, :, rows, cols], down, right)

    band = lambda down: jnp.concatenate([got(down, 1), got(down, 0), got(down, -1)], axis=3)
    middle = jnp.concatenate([got(0, 1), tile_data, got(0, -1)], axis=3)
    return jnp.concatenate([band(1), middle, band(-1)], axis=2)


def fold_halo(canvas, half):
    size = canvas.shape[-1] - 2 * half
    parts = {1: slice(half + size, 2 * half + size), 0: slice(half, half + size), -1: slice(0, half)}
    places = {1: slice(0, half), 0: slice(0, size), -1: slice(size - half, size)}
    core = canvas[:, :, half : half + size, half : half + size]
    for down in (1, 0, -1):
        for right in (1, 0, -1):
            if down == 0 and right == 0:
                continue
            piece = from_neighbour(canvas[:, :, parts[down], parts[right]], down, right)
            spots = [places[down], places[right]]
            widths = [(spot.start, size - spot.stop) for spot in spots]
            core = core + jnp.pad(piece, [(0, 0), (0, 0)] + widths)
    return core


def shards(object_slices, probe, fresnel_phase, intensity, offsets, counts):
    patch = probe.shape[-1]
    half = patch // 2
    tile = object_slices.shape[-1]
    layers = object_slices.shape[0]
    basis_re, basis_im = dft_basis(patch)
    kernel_re = jnp.cos(fresnel_phase)
    kernel_im = jnp.sin(fresnel_phase)
    measured = intensity[0, 0]
    places = offsets[0, 0] + half
    window_shape = (layers, 2, patch, patch)
    zero_index = jnp.zeros((), jnp.int32)
    padded = with_halo(object_slices, half)
    row_here = lax.axis_index("ty")
    col_here = lax.axis_index("tx")
    mine = counts[row_here, col_here]

    def start_of(slot):
        return (zero_index, zero_index, places[slot, 0], places[slot, 1])

    def window_at(slot):
        return lax.dynamic_slice(padded, start_of(slot), window_shape)

    plain = (
        jnp.concatenate([basis_re, basis_im], axis=0),
        jnp.concatenate([basis_re, basis_im], axis=1),
    )
    conjugate = (
        jnp.concatenate([basis_re, -basis_im], axis=0),
        jnp.concatenate([basis_re, -basis_im], axis=1),
    )
    slots = measured.shape[0]
    windows = jnp.stack([window_at(slot) for slot in range(slots)])
    terms = batched_grad(windows, measured, probe, kernel_re, kernel_im, plain, conjugate)
    span = tile + 2 * half
    block = patch + half
    last_block = (span - block) // half

    def add_at(gradient, slot, term):
        row, col = (places[slot, 0], places[slot, 1])
        block_row = jnp.minimum(row // half, last_block)
        block_col = jnp.minimum(col // half, last_block)
        term = jnp.where(slot < mine, term, jnp.zeros_like(term))
        spread = jnp.pad(term, ((0, 0), (0, 0), (half, half), (half, half)))
        inner = (zero_index, zero_index, half - (row - block_row * half), half - (col - block_col * half))
        shifted = lax.dynamic_slice(spread, inner, (layers, 2, block, block))
        start = (zero_index, zero_index, block_row * half, block_col * half)
        current = lax.dynamic_slice(gradient, start, shifted.shape)
        return lax.dynamic_update_slice(gradient, current + shifted, start)

    gradient = jnp.zeros((layers, 2, span, span), jnp.float32)
    for slot in range(slots):
        gradient = add_at(gradient, slot, terms[slot])
    core = fold_halo(gradient, half)
    return object_slices - STEP_SIZE * core


def solution(mesh):
    placed = (
        P(None, None, "ty", "tx"),
        P(),
        P(),
        P("ty", "tx", None, None, None),
        P("ty", "tx", None, None),
        P(),
    )
    return jax.shard_map(
        shards, mesh=mesh, in_specs=placed, out_specs=P(None, None, "ty", "tx"), check_vma=False
    )
```

```python
import math

import jax
import jax.numpy as jnp
from jax import lax
from jax.sharding import PartitionSpec as P

HIGH = lax.Precision.HIGHEST
FAST = lax.Precision.HIGH
STEP_SIZE = 0.25


def dft_basis(length):
    index = jnp.arange(length, dtype=jnp.int32)
    turns = index[:, None] * index[None, :] % length
    angles = turns.astype(jnp.float32) * (2.0 * math.pi / length)
    scale = 1.0 / math.sqrt(length)
    return (jnp.cos(angles) * scale, -jnp.sin(angles) * scale)


def matmul_high(left, right):
    return jnp.dot(left, right, precision=HIGH, preferred_element_type=jnp.float32)


def complex_matmul(left_re, left_im, right_re, right_im):
    real = matmul_high(left_re, right_re) - matmul_high(left_im, right_im)
    imag = matmul_high(left_re, right_im) + matmul_high(left_im, right_re)
    return (real, imag)


def forward_dft(field_re, field_im, basis_re, basis_im):
    temp_re, temp_im = complex_matmul(basis_re, basis_im, field_re, field_im)
    return complex_matmul(temp_re, temp_im, basis_re, basis_im)


def complex_times(left_re, left_im, right_re, right_im):
    return (left_re * right_re - left_im * right_im, left_re * right_im + left_im * right_re)


def conj_times(left_re, left_im, right_re, right_im):
    return (left_re * right_re + left_im * right_im, left_im * right_re - left_re * right_im)


def matmul_fast(left, right):
    return jnp.dot(left, right, precision=FAST, preferred_element_type=jnp.float32)


def right_times(field_re, field_im, basis):
    count = field_re.shape[0]
    side = basis.shape[0]
    stacked = jnp.concatenate([field_re, field_im], axis=0)
    both = jnp.einsum("bjk,kl->bjl", stacked, basis, precision=FAST, preferred_element_type=jnp.float32)
    real = both[:count, :, :side] - both[count:, :, side:]
    imag = both[:count, :, side:] + both[count:, :, :side]
    return (real, imag)


def left_times(basis, field_re, field_im):
    side = basis.shape[1]
    stacked = jnp.concatenate([field_re, field_im], axis=2)
    both = jnp.stack([matmul_fast(basis, one) for one in stacked])
    real = both[:, :side, :side] - both[:, side:, side:]
    imag = both[:, :side, side:] + both[:, side:, :side]
    return (real, imag)


def two_sided(field_re, field_im, bases):
    left, right = bases
    temp_re, temp_im = left_times(left, field_re, field_im)
    return right_times(temp_re, temp_im, right)


def batched_grad(window, measured, probe, kernel_re, kernel_im, plain, conjugate):
    first_re, first_im = complex_times(probe[0], probe[1], window[:, 0, 0], window[:, 0, 1])
    spec_re, spec_im = two_sided(first_re, first_im, plain)
    spec_re, spec_im = complex_times(kernel_re, kernel_im, spec_re, spec_im)
    phi_re, phi_im = two_sided(spec_re, spec_im, conjugate)
    exit_re, exit_im = complex_times(phi_re, phi_im, window[:, 1, 0], window[:, 1, 1])
    far_re, far_im = two_sided(exit_re, exit_im, plain)
    misfit = far_re * far_re + far_im * far_im - measured
    back_re, back_im = two_sided(misfit * far_re, misfit * far_im, conjugate)
    second_re, second_im = conj_times(back_re, back_im, phi_re, phi_im)
    wave_re, wave_im = conj_times(back_re, back_im, window[:, 1, 0], window[:, 1, 1])
    wave_re, wave_im = two_sided(wave_re, wave_im, plain)
    wave_re, wave_im = conj_times(wave_re, wave_im, kernel_re, kernel_im)
    wave_re, wave_im = two_sided(wave_re, wave_im, conjugate)
    lead_re, lead_im = conj_times(wave_re, wave_im, probe[0], probe[1])
    return jnp.stack([jnp.stack([lead_re, lead_im], 1), jnp.stack([second_re, second_im], 1)], 1)


def passed_along(value, axis, steps):
    count = lax.axis_size(axis)
    first, last = (max(0, -steps), min(count, count - steps))
    return lax.ppermute(value, axis, [(source, source + steps) for source in range(first, last)])


def with_halo(tile_data, half):
    for axis, dim in (("ty", 2), ("tx", 3)):
        length = tile_data.shape[dim]
        before = passed_along(lax.slice_in_dim(tile_data, length - half, length, axis=dim), axis, 1)
        after = passed_along(lax.slice_in_dim(tile_data, 0, half, axis=dim), axis, -1)
        tile_data = jnp.concatenate([before, tile_data, after], axis=dim)
    return tile_data


def fold_halo(canvas, half):
    for axis, dim in (("tx", 3), ("ty", 2)):
        length = canvas.shape[dim]
        size = length - 2 * half
        inner = lax.slice_in_dim(canvas, half, half + size, axis=dim)
        late = passed_along(lax.slice_in_dim(canvas, half + size, length, axis=dim), axis, 1)
        early = passed_along(lax.slice_in_dim(canvas, 0, half, axis=dim), axis, -1)
        widths = [(0, 0)] * canvas.ndim
        widths[dim] = (0, size - half)
        inner = inner + jnp.pad(late, widths)
        widths[dim] = (size - half, 0)
        canvas = inner + jnp.pad(early, widths)
    return canvas


def shards(object_slices, probe, fresnel_phase, intensity, offsets, counts):
    patch = probe.shape[-1]
    half = patch // 2
    tile = object_slices.shape[-1]
    layers = object_slices.shape[0]
    basis_re, basis_im = dft_basis(patch)
    kernel_re = jnp.cos(fresnel_phase)
    kernel_im = jnp.sin(fresnel_phase)
    measured = intensity[0, 0]
    places = offsets[0, 0] + half
    window_shape = (layers, 2, patch, patch)
    zero_index = jnp.zeros((), jnp.int32)
    padded = with_halo(object_slices, half)
    row_here = lax.axis_index("ty")
    col_here = lax.axis_index("tx")
    mine = counts[row_here, col_here]

    def start_of(slot):
        return (zero_index, zero_index, places[slot, 0], places[slot, 1])

    def window_at(slot):
        return lax.dynamic_slice(padded, start_of(slot), window_shape)

    plain = (
        jnp.concatenate([basis_re, basis_im], axis=0),
        jnp.concatenate([basis_re, basis_im], axis=1),
    )
    conjugate = (
        jnp.concatenate([basis_re, -basis_im], axis=0),
        jnp.concatenate([basis_re, -basis_im], axis=1),
    )
    slots = measured.shape[0]
    windows = jnp.stack([window_at(slot) for slot in range(slots)])
    terms = batched_grad(windows, measured, probe, kernel_re, kernel_im, plain, conjugate)
    span = tile + 2 * half
    block = patch + half
    last_block = (span - block) // half

    def add_at(gradient, slot, term):
        row, col = (places[slot, 0], places[slot, 1])
        block_row = jnp.minimum(row // half, last_block)
        block_col = jnp.minimum(col // half, last_block)
        term = jnp.where(slot < mine, term, jnp.zeros_like(term))
        spread = jnp.pad(term, ((0, 0), (0, 0), (half, half), (half, half)))
        inner = (zero_index, zero_index, half - (row - block_row * half), half - (col - block_col * half))
        shifted = lax.dynamic_slice(spread, inner, (layers, 2, block, block))
        start = (zero_index, zero_index, block_row * half, block_col * half)
        current = lax.dynamic_slice(gradient, start, shifted.shape)
        return lax.dynamic_update_slice(gradient, current + shifted, start)

    gradient = jnp.zeros((layers, 2, span, span), jnp.float32)
    for slot in range(slots):
        gradient = add_at(gradient, slot, terms[slot])
    core = fold_halo(gradient, half)
    return object_slices - STEP_SIZE * core


def solution(mesh):
    placed = (
        P(None, None, "ty", "tx"),
        P(),
        P(),
        P("ty", "tx", None, None, None),
        P("ty", "tx", None, None),
        P(),
    )
    return jax.shard_map(
        shards, mesh=mesh, in_specs=placed, out_specs=P(None, None, "ty", "tx"), check_vma=False
    )
```

```python
import math

import jax
import jax.numpy as jnp
from jax import lax
from jax.sharding import PartitionSpec as P

HIGH = lax.Precision.HIGHEST
FAST = lax.Precision.HIGH
STEP_SIZE = 0.25


def dft_basis(length):
    index = jnp.arange(length, dtype=jnp.int32)
    turns = index[:, None] * index[None, :] % length
    angles = turns.astype(jnp.float32) * (2.0 * math.pi / length)
    scale = 1.0 / math.sqrt(length)
    return (jnp.cos(angles) * scale, -jnp.sin(angles) * scale)


def matmul_high(left, right):
    return jnp.dot(left, right, precision=HIGH, preferred_element_type=jnp.float32)


def complex_matmul(left_re, left_im, right_re, right_im):
    real = matmul_high(left_re, right_re) - matmul_high(left_im, right_im)
    imag = matmul_high(left_re, right_im) + matmul_high(left_im, right_re)
    return (real, imag)


def forward_dft(field_re, field_im, basis_re, basis_im):
    temp_re, temp_im = complex_matmul(basis_re, basis_im, field_re, field_im)
    return complex_matmul(temp_re, temp_im, basis_re, basis_im)


def complex_times(left_re, left_im, right_re, right_im):
    return (left_re * right_re - left_im * right_im, left_re * right_im + left_im * right_re)


def conj_times(left_re, left_im, right_re, right_im):
    return (left_re * right_re + left_im * right_im, left_im * right_re - left_re * right_im)


def matmul_fast(left, right):
    return jnp.dot(left, right, precision=FAST, preferred_element_type=jnp.float32)


def right_times(field_re, field_im, basis):
    count = field_re.shape[0]
    side = basis.shape[0]
    stacked = jnp.concatenate([field_re, field_im], axis=0)
    both = jnp.einsum("bjk,kl->bjl", stacked, basis, precision=FAST, preferred_element_type=jnp.float32)
    real = both[:count, :, :side] - both[count:, :, side:]
    imag = both[:count, :, side:] + both[count:, :, :side]
    return (real, imag)


def left_times(basis, field_re, field_im):
    side = basis.shape[1]
    stacked = jnp.concatenate([field_re, field_im], axis=2)
    both = jnp.stack([matmul_fast(basis, one) for one in stacked])
    real = both[:, :side, :side] - both[:, side:, side:]
    imag = both[:, :side, side:] + both[:, side:, :side]
    return (real, imag)


def two_sided(field_re, field_im, bases):
    left, right = bases
    temp_re, temp_im = left_times(left, field_re, field_im)
    return right_times(temp_re, temp_im, right)


def batched_grad(window, measured, probe, kernel_re, kernel_im, plain, conjugate):
    first_re, first_im = complex_times(probe[0], probe[1], window[:, 0, 0], window[:, 0, 1])
    spec_re, spec_im = two_sided(first_re, first_im, plain)
    spec_re, spec_im = complex_times(kernel_re, kernel_im, spec_re, spec_im)
    phi_re, phi_im = two_sided(spec_re, spec_im, conjugate)
    exit_re, exit_im = complex_times(phi_re, phi_im, window[:, 1, 0], window[:, 1, 1])
    far_re, far_im = two_sided(exit_re, exit_im, plain)
    misfit = far_re * far_re + far_im * far_im - measured
    back_re, back_im = two_sided(misfit * far_re, misfit * far_im, conjugate)
    second_re, second_im = conj_times(back_re, back_im, phi_re, phi_im)
    wave_re, wave_im = conj_times(back_re, back_im, window[:, 1, 0], window[:, 1, 1])
    wave_re, wave_im = two_sided(wave_re, wave_im, plain)
    wave_re, wave_im = conj_times(wave_re, wave_im, kernel_re, kernel_im)
    wave_re, wave_im = two_sided(wave_re, wave_im, conjugate)
    lead_re, lead_im = conj_times(wave_re, wave_im, probe[0], probe[1])
    return jnp.stack([jnp.stack([lead_re, lead_im], 1), jnp.stack([second_re, second_im], 1)], 1)


def passed_along(value, axis, steps):
    count = lax.axis_size(axis)
    first, last = (max(0, -steps), min(count, count - steps))
    return lax.ppermute(value, axis, [(source, source + steps) for source in range(first, last)])


def neighbour_pairs(rows, cols, down, right):
    pairs = []
    for row in range(rows):
        for col in range(cols):
            to_row, to_col = (row + down, col + right)
            if 0 <= to_row < rows and 0 <= to_col < cols:
                pairs.append((row * cols + col, to_row * cols + to_col))
    return pairs


def from_neighbour(piece, down, right):
    rows, cols = (lax.axis_size("ty"), lax.axis_size("tx"))
    return lax.ppermute(piece, ("ty", "tx"), neighbour_pairs(rows, cols, down, right))


def with_halo(tile_data, half):
    size = tile_data.shape[-1]
    low, high = (slice(0, half), slice(size - half, size))
    every = slice(None)

    def got(down, right):
        rows = {1: high, 0: every, -1: low}[down]
        cols = {1: high, 0: every, -1: low}[right]
        return from_neighbour(tile_data[:, :, rows, cols], down, right)

    band = lambda down: jnp.concatenate([got(down, 1), got(down, 0), got(down, -1)], axis=3)
    middle = jnp.concatenate([got(0, 1), tile_data, got(0, -1)], axis=3)
    return jnp.concatenate([band(1), middle, band(-1)], axis=2)


def fold_halo(canvas, half):
    for axis, dim in (("tx", 3), ("ty", 2)):
        length = canvas.shape[dim]
        size = length - 2 * half
        inner = lax.slice_in_dim(canvas, half, half + size, axis=dim)
        late = passed_along(lax.slice_in_dim(canvas, half + size, length, axis=dim), axis, 1)
        early = passed_along(lax.slice_in_dim(canvas, 0, half, axis=dim), axis, -1)
        widths = [(0, 0)] * canvas.ndim
        widths[dim] = (0, size - half)
        inner = inner + jnp.pad(late, widths)
        widths[dim] = (size - half, 0)
        canvas = inner + jnp.pad(early, widths)
    return canvas


def shards(object_slices, probe, fresnel_phase, intensity, offsets, counts):
    patch = probe.shape[-1]
    half = patch // 2
    tile = object_slices.shape[-1]
    layers = object_slices.shape[0]
    basis_re, basis_im = dft_basis(patch)
    kernel_re = jnp.cos(fresnel_phase)
    kernel_im = jnp.sin(fresnel_phase)
    measured = intensity[0, 0]
    places = offsets[0, 0] + half
    window_shape = (layers, 2, patch, patch)
    zero_index = jnp.zeros((), jnp.int32)
    padded = with_halo(object_slices, half)
    row_here = lax.axis_index("ty")
    col_here = lax.axis_index("tx")
    mine = counts[row_here, col_here]

    def start_of(slot):
        return (zero_index, zero_index, places[slot, 0], places[slot, 1])

    def window_at(slot):
        return lax.dynamic_slice(padded, start_of(slot), window_shape)

    plain = (
        jnp.concatenate([basis_re, basis_im], axis=0),
        jnp.concatenate([basis_re, basis_im], axis=1),
    )
    conjugate = (
        jnp.concatenate([basis_re, -basis_im], axis=0),
        jnp.concatenate([basis_re, -basis_im], axis=1),
    )
    slots = measured.shape[0]
    windows = jnp.stack([window_at(slot) for slot in range(slots)])
    terms = batched_grad(windows, measured, probe, kernel_re, kernel_im, plain, conjugate)
    span = tile + 2 * half
    block = patch + half
    last_block = (span - block) // half

    def add_at(gradient, slot, term):
        row, col = (places[slot, 0], places[slot, 1])
        block_row = jnp.minimum(row // half, last_block)
        block_col = jnp.minimum(col // half, last_block)
        term = jnp.where(slot < mine, term, jnp.zeros_like(term))
        spread = jnp.pad(term, ((0, 0), (0, 0), (half, half), (half, half)))
        inner = (zero_index, zero_index, half - (row - block_row * half), half - (col - block_col * half))
        shifted = lax.dynamic_slice(spread, inner, (layers, 2, block, block))
        start = (zero_index, zero_index, block_row * half, block_col * half)
        current = lax.dynamic_slice(gradient, start, shifted.shape)
        return lax.dynamic_update_slice(gradient, current + shifted, start)

    gradient = jnp.zeros((layers, 2, span, span), jnp.float32)
    for slot in range(slots):
        gradient = add_at(gradient, slot, terms[slot])
    core = fold_halo(gradient, half)
    return object_slices - STEP_SIZE * core


def solution(mesh):
    placed = (
        P(None, None, "ty", "tx"),
        P(),
        P(),
        P("ty", "tx", None, None, None),
        P("ty", "tx", None, None),
        P(),
    )
    return jax.shard_map(
        shards, mesh=mesh, in_specs=placed, out_specs=P(None, None, "ty", "tx"), check_vma=False
    )
```

```python
import math

import jax
import jax.numpy as jnp
from jax import lax
from jax.sharding import PartitionSpec as P

HIGH = lax.Precision.HIGHEST
FAST = lax.Precision.HIGH
STEP_SIZE = 0.25


def dft_basis(length):
    index = jnp.arange(length, dtype=jnp.int32)
    turns = index[:, None] * index[None, :] % length
    angles = turns.astype(jnp.float32) * (2.0 * math.pi / length)
    scale = 1.0 / math.sqrt(length)
    return (jnp.cos(angles) * scale, -jnp.sin(angles) * scale)


def matmul_high(left, right):
    return jnp.dot(left, right, precision=HIGH, preferred_element_type=jnp.float32)


def complex_matmul(left_re, left_im, right_re, right_im):
    real = matmul_high(left_re, right_re) - matmul_high(left_im, right_im)
    imag = matmul_high(left_re, right_im) + matmul_high(left_im, right_re)
    return (real, imag)


def forward_dft(field_re, field_im, basis_re, basis_im):
    temp_re, temp_im = complex_matmul(basis_re, basis_im, field_re, field_im)
    return complex_matmul(temp_re, temp_im, basis_re, basis_im)


def complex_times(left_re, left_im, right_re, right_im):
    return (left_re * right_re - left_im * right_im, left_re * right_im + left_im * right_re)


def conj_times(left_re, left_im, right_re, right_im):
    return (left_re * right_re + left_im * right_im, left_im * right_re - left_re * right_im)


def matmul_fast(left, right):
    return jnp.dot(left, right, precision=FAST, preferred_element_type=jnp.float32)


def right_times(field_re, field_im, basis):
    count = field_re.shape[0]
    side = basis.shape[0]
    stacked = jnp.concatenate([field_re, field_im], axis=0)
    both = jnp.einsum("bjk,kl->bjl", stacked, basis, precision=FAST, preferred_element_type=jnp.float32)
    real = both[:count, :, :side] - both[count:, :, side:]
    imag = both[:count, :, side:] + both[count:, :, :side]
    return (real, imag)


def left_times(basis, field_re, field_im):
    side = basis.shape[1]
    stacked = jnp.concatenate([field_re, field_im], axis=2)
    both = jnp.stack([matmul_fast(basis, one) for one in stacked])
    real = both[:, :side, :side] - both[:, side:, side:]
    imag = both[:, :side, side:] + both[:, side:, :side]
    return (real, imag)


def two_sided(field_re, field_im, bases):
    left, right = bases
    temp_re, temp_im = left_times(left, field_re, field_im)
    return right_times(temp_re, temp_im, right)


def batched_grad(window, measured, probe, kernel_re, kernel_im, plain, conjugate):
    first_re, first_im = complex_times(probe[0], probe[1], window[:, 0, 0], window[:, 0, 1])
    spec_re, spec_im = two_sided(first_re, first_im, plain)
    spec_re, spec_im = complex_times(kernel_re, kernel_im, spec_re, spec_im)
    phi_re, phi_im = two_sided(spec_re, spec_im, conjugate)
    exit_re, exit_im = complex_times(phi_re, phi_im, window[:, 1, 0], window[:, 1, 1])
    far_re, far_im = two_sided(exit_re, exit_im, plain)
    misfit = far_re * far_re + far_im * far_im - measured
    back_re, back_im = two_sided(misfit * far_re, misfit * far_im, conjugate)
    second_re, second_im = conj_times(back_re, back_im, phi_re, phi_im)
    wave_re, wave_im = conj_times(back_re, back_im, window[:, 1, 0], window[:, 1, 1])
    wave_re, wave_im = two_sided(wave_re, wave_im, plain)
    wave_re, wave_im = conj_times(wave_re, wave_im, kernel_re, kernel_im)
    wave_re, wave_im = two_sided(wave_re, wave_im, conjugate)
    lead_re, lead_im = conj_times(wave_re, wave_im, probe[0], probe[1])
    return jnp.stack([jnp.stack([lead_re, lead_im], 1), jnp.stack([second_re, second_im], 1)], 1)


def passed_along(value, axis, steps):
    count = lax.axis_size(axis)
    first, last = (max(0, -steps), min(count, count - steps))
    return lax.ppermute(value, axis, [(source, source + steps) for source in range(first, last)])


def with_halo(tile_data, half):
    top = passed_along(tile_data[:, :, -half:], "ty", 1)
    bottom = passed_along(tile_data[:, :, :half], "ty", -1)
    left = passed_along(tile_data[..., -half:], "tx", 1)
    right = passed_along(tile_data[..., :half], "tx", -1)
    ends = jnp.concatenate([top, bottom], axis=2)
    from_left = passed_along(ends[..., -half:], "tx", 1)
    from_right = passed_along(ends[..., :half], "tx", -1)
    rows = [
        jnp.concatenate([from_left[:, :, :half], top, from_right[:, :, :half]], axis=3),
        jnp.concatenate([left, tile_data, right], axis=3),
        jnp.concatenate([from_left[:, :, half:], bottom, from_right[:, :, half:]], axis=3),
    ]
    return jnp.concatenate(rows, axis=2)


def placed(piece, rows, cols, size):
    widths = [(0, 0), (0, 0), (rows, size - rows - piece.shape[2]), (cols, size - cols - piece.shape[3])]
    return jnp.pad(piece, widths)


def fold_halo(canvas, half):
    size = canvas.shape[-1] - 2 * half
    inner = slice(half, half + size)
    from_left = passed_along(canvas[..., half + size :], "tx", 1)
    from_right = passed_along(canvas[..., :half], "tx", -1)
    from_above = passed_along(canvas[:, :, half + size :, inner], "ty", 1)
    from_below = passed_along(canvas[:, :, :half, inner], "ty", -1)
    upward = jnp.concatenate([from_left[:, :, :half], from_right[:, :, :half]], axis=3)
    downward = jnp.concatenate([from_left[:, :, half + size :], from_right[:, :, half + size :]], axis=3)
    relayed_below = passed_along(upward, "ty", -1)
    relayed_above = passed_along(downward, "ty", 1)
    far = size - half
    core = canvas[:, :, inner, inner]
    core = core + placed(from_left[:, :, inner], 0, 0, size) + placed(from_right[:, :, inner], 0, far, size)
    core = core + placed(from_above, 0, 0, size) + placed(from_below, far, 0, size)
    core = core + placed(relayed_above[..., :half], 0, 0, size) + placed(relayed_above[..., half:], 0, far, size)
    core = core + placed(relayed_below[..., :half], far, 0, size) + placed(relayed_below[..., half:], far, far, size)
    return core


def shards(object_slices, probe, fresnel_phase, intensity, offsets, counts):
    patch = probe.shape[-1]
    half = patch // 2
    tile = object_slices.shape[-1]
    layers = object_slices.shape[0]
    basis_re, basis_im = dft_basis(patch)
    kernel_re = jnp.cos(fresnel_phase)
    kernel_im = jnp.sin(fresnel_phase)
    measured = intensity[0, 0]
    places = offsets[0, 0] + half
    window_shape = (layers, 2, patch, patch)
    zero_index = jnp.zeros((), jnp.int32)
    padded = with_halo(object_slices, half)
    row_here = lax.axis_index("ty")
    col_here = lax.axis_index("tx")
    mine = counts[row_here, col_here]

    def start_of(slot):
        return (zero_index, zero_index, places[slot, 0], places[slot, 1])

    def window_at(slot):
        return lax.dynamic_slice(padded, start_of(slot), window_shape)

    plain = (
        jnp.concatenate([basis_re, basis_im], axis=0),
        jnp.concatenate([basis_re, basis_im], axis=1),
    )
    conjugate = (
        jnp.concatenate([basis_re, -basis_im], axis=0),
        jnp.concatenate([basis_re, -basis_im], axis=1),
    )
    slots = measured.shape[0]
    windows = jnp.stack([window_at(slot) for slot in range(slots)])
    terms = batched_grad(windows, measured, probe, kernel_re, kernel_im, plain, conjugate)
    span = tile + 2 * half
    block = patch + half
    last_block = (span - block) // half

    def add_at(gradient, slot, term):
        row, col = (places[slot, 0], places[slot, 1])
        block_row = jnp.minimum(row // half, last_block)
        block_col = jnp.minimum(col // half, last_block)
        term = jnp.where(slot < mine, term, jnp.zeros_like(term))
        spread = jnp.pad(term, ((0, 0), (0, 0), (half, half), (half, half)))
        inner = (zero_index, zero_index, half - (row - block_row * half), half - (col - block_col * half))
        shifted = lax.dynamic_slice(spread, inner, (layers, 2, block, block))
        start = (zero_index, zero_index, block_row * half, block_col * half)
        current = lax.dynamic_slice(gradient, start, shifted.shape)
        return lax.dynamic_update_slice(gradient, current + shifted, start)

    gradient = jnp.zeros((layers, 2, span, span), jnp.float32)
    for slot in range(slots):
        gradient = add_at(gradient, slot, terms[slot])
    core = fold_halo(gradient, half)
    return object_slices - STEP_SIZE * core


def solution(mesh):
    placed = (
        P(None, None, "ty", "tx"),
        P(),
        P(),
        P("ty", "tx", None, None, None),
        P("ty", "tx", None, None),
        P(),
    )
    return jax.shard_map(
        shards, mesh=mesh, in_specs=placed, out_specs=P(None, None, "ty", "tx"), check_vma=False
    )
```

```python
import math

import jax
import jax.numpy as jnp
from jax import lax
from jax.sharding import PartitionSpec as P

HIGH = lax.Precision.HIGHEST
FAST = lax.Precision.HIGH
STEP_SIZE = 0.25


def dft_basis(length):
    index = jnp.arange(length, dtype=jnp.int32)
    turns = index[:, None] * index[None, :] % length
    angles = turns.astype(jnp.float32) * (2.0 * math.pi / length)
    scale = 1.0 / math.sqrt(length)
    return (jnp.cos(angles) * scale, -jnp.sin(angles) * scale)


def matmul_high(left, right):
    return jnp.dot(left, right, precision=HIGH, preferred_element_type=jnp.float32)


def complex_matmul(left_re, left_im, right_re, right_im):
    real = matmul_high(left_re, right_re) - matmul_high(left_im, right_im)
    imag = matmul_high(left_re, right_im) + matmul_high(left_im, right_re)
    return (real, imag)


def forward_dft(field_re, field_im, basis_re, basis_im):
    temp_re, temp_im = complex_matmul(basis_re, basis_im, field_re, field_im)
    return complex_matmul(temp_re, temp_im, basis_re, basis_im)


def complex_times(left_re, left_im, right_re, right_im):
    return (left_re * right_re - left_im * right_im, left_re * right_im + left_im * right_re)


def conj_times(left_re, left_im, right_re, right_im):
    return (left_re * right_re + left_im * right_im, left_im * right_re - left_re * right_im)


def matmul_fast(left, right):
    return jnp.dot(left, right, precision=FAST, preferred_element_type=jnp.float32)


def right_times(field_re, field_im, basis):
    count = field_re.shape[0]
    side = basis.shape[0]
    stacked = jnp.concatenate([field_re, field_im], axis=0)
    both = jnp.einsum("bjk,kl->bjl", stacked, basis, precision=FAST, preferred_element_type=jnp.float32)
    real = both[:count, :, :side] - both[count:, :, side:]
    imag = both[:count, :, side:] + both[count:, :, :side]
    return (real, imag)


def left_times(basis, field_re, field_im):
    side = basis.shape[1]
    stacked = jnp.concatenate([field_re, field_im], axis=2)
    both = jnp.stack([matmul_fast(basis, one) for one in stacked])
    real = both[:, :side, :side] - both[:, side:, side:]
    imag = both[:, :side, side:] + both[:, side:, :side]
    return (real, imag)


def two_sided(field_re, field_im, bases):
    left, right = bases
    temp_re, temp_im = left_times(left, field_re, field_im)
    return right_times(temp_re, temp_im, right)


def batched_grad(front, back, measured, probe, kernel_re, kernel_im, plain, conjugate):
    first_re, first_im = complex_times(probe[0], probe[1], front[:, 0], front[:, 1])
    spec_re, spec_im = two_sided(first_re, first_im, plain)
    spec_re, spec_im = complex_times(kernel_re, kernel_im, spec_re, spec_im)
    phi_re, phi_im = two_sided(spec_re, spec_im, conjugate)
    exit_re, exit_im = complex_times(phi_re, phi_im, back[:, 0], back[:, 1])
    far_re, far_im = two_sided(exit_re, exit_im, plain)
    misfit = far_re * far_re + far_im * far_im - measured
    return_re, return_im = two_sided(misfit * far_re, misfit * far_im, conjugate)
    second_re, second_im = conj_times(return_re, return_im, phi_re, phi_im)
    wave_re, wave_im = conj_times(return_re, return_im, back[:, 0], back[:, 1])
    wave_re, wave_im = two_sided(wave_re, wave_im, plain)
    wave_re, wave_im = conj_times(wave_re, wave_im, kernel_re, kernel_im)
    wave_re, wave_im = two_sided(wave_re, wave_im, conjugate)
    lead_re, lead_im = conj_times(wave_re, wave_im, probe[0], probe[1])
    return (jnp.stack([lead_re, lead_im], 1), jnp.stack([second_re, second_im], 1))


def passed_along(value, axis, steps):
    count = lax.axis_size(axis)
    first, last = (max(0, -steps), min(count, count - steps))
    return lax.ppermute(value, axis, [(source, source + steps) for source in range(first, last)])


def with_halo(tile_data, half):
    for axis, dim in (("ty", 2), ("tx", 3)):
        length = tile_data.shape[dim]
        before = passed_along(lax.slice_in_dim(tile_data, length - half, length, axis=dim), axis, 1)
        after = passed_along(lax.slice_in_dim(tile_data, 0, half, axis=dim), axis, -1)
        tile_data = jnp.concatenate([before, tile_data, after], axis=dim)
    return tile_data


def fold_halo(canvas, half):
    for axis, dim in (("tx", 3), ("ty", 2)):
        length = canvas.shape[dim]
        size = length - 2 * half
        inner = lax.slice_in_dim(canvas, half, half + size, axis=dim)
        late = passed_along(lax.slice_in_dim(canvas, half + size, length, axis=dim), axis, 1)
        early = passed_along(lax.slice_in_dim(canvas, 0, half, axis=dim), axis, -1)
        widths = [(0, 0)] * canvas.ndim
        widths[dim] = (0, size - half)
        inner = inner + jnp.pad(late, widths)
        widths[dim] = (size - half, 0)
        canvas = inner + jnp.pad(early, widths)
    return canvas


def shards(object_slices, probe, fresnel_phase, intensity, offsets, counts):
    patch = probe.shape[-1]
    half = patch // 2
    tile = object_slices.shape[-1]
    layers = object_slices.shape[0]
    basis_re, basis_im = dft_basis(patch)
    kernel_re = jnp.cos(fresnel_phase)
    kernel_im = jnp.sin(fresnel_phase)
    measured = intensity[0, 0]
    places = offsets[0, 0] + half
    window_shape = (1, 2, patch, patch)
    zero_index = jnp.zeros((), jnp.int32)
    row_here = lax.axis_index("ty")
    col_here = lax.axis_index("tx")
    mine = counts[row_here, col_here]
    plain = (
        jnp.concatenate([basis_re, basis_im], axis=0),
        jnp.concatenate([basis_re, basis_im], axis=1),
    )
    conjugate = (
        jnp.concatenate([basis_re, -basis_im], axis=0),
        jnp.concatenate([basis_re, -basis_im], axis=1),
    )
    slots = measured.shape[0]

    def start_of(slot):
        return (zero_index, zero_index, places[slot, 0], places[slot, 1])

    def windows_of(layer):
        padded = with_halo(object_slices[layer : layer + 1], half)
        return jnp.stack([lax.dynamic_slice(padded, start_of(slot), window_shape)[0] for slot in range(slots)])

    span = tile + 2 * half
    block = patch + half
    last_block = (span - block) // half

    def add_at(gradient, slot, term):
        row, col = (places[slot, 0], places[slot, 1])
        block_row = jnp.minimum(row // half, last_block)
        block_col = jnp.minimum(col // half, last_block)
        term = jnp.where(slot < mine, term, jnp.zeros_like(term))
        spread = jnp.pad(term, ((0, 0), (half, half), (half, half)))
        inner = (zero_index, half - (row - block_row * half), half - (col - block_col * half))
        shifted = lax.dynamic_slice(spread, inner, (2, block, block))
        start = (zero_index, block_row * half, block_col * half)
        current = lax.dynamic_slice(gradient, start, shifted.shape)
        return lax.dynamic_update_slice(gradient, current + shifted, start)

    def folded(terms):
        gradient = jnp.zeros((2, span, span), jnp.float32)
        for slot in range(slots):
            gradient = add_at(gradient, slot, terms[slot])
        return fold_halo(gradient[None], half)[0]

    lead, second = batched_grad(windows_of(0), windows_of(1), measured, probe, kernel_re, kernel_im, plain, conjugate)
    core = jnp.stack([folded(lead), folded(second)])
    return object_slices - STEP_SIZE * core


def solution(mesh):
    placed = (
        P(None, None, "ty", "tx"),
        P(),
        P(),
        P("ty", "tx", None, None, None),
        P("ty", "tx", None, None),
        P(),
    )
    return jax.shard_map(
        shards, mesh=mesh, in_specs=placed, out_specs=P(None, None, "ty", "tx"), check_vma=False
    )
```

```python
import math

import jax
import jax.numpy as jnp
from jax import lax
from jax.sharding import PartitionSpec as P

HIGH = lax.Precision.HIGHEST
FAST = lax.Precision.HIGH
STEP_SIZE = 0.25


def dft_basis(length):
    index = jnp.arange(length, dtype=jnp.int32)
    turns = index[:, None] * index[None, :] % length
    angles = turns.astype(jnp.float32) * (2.0 * math.pi / length)
    scale = 1.0 / math.sqrt(length)
    return (jnp.cos(angles) * scale, -jnp.sin(angles) * scale)


def matmul_high(left, right):
    return jnp.dot(left, right, precision=HIGH, preferred_element_type=jnp.float32)


def complex_matmul(left_re, left_im, right_re, right_im):
    real = matmul_high(left_re, right_re) - matmul_high(left_im, right_im)
    imag = matmul_high(left_re, right_im) + matmul_high(left_im, right_re)
    return (real, imag)


def forward_dft(field_re, field_im, basis_re, basis_im):
    temp_re, temp_im = complex_matmul(basis_re, basis_im, field_re, field_im)
    return complex_matmul(temp_re, temp_im, basis_re, basis_im)


def complex_times(left_re, left_im, right_re, right_im):
    return (left_re * right_re - left_im * right_im, left_re * right_im + left_im * right_re)


def conj_times(left_re, left_im, right_re, right_im):
    return (left_re * right_re + left_im * right_im, left_im * right_re - left_re * right_im)


def matmul_fast(left, right):
    return jnp.dot(left, right, precision=FAST, preferred_element_type=jnp.float32)


def right_times(field_re, field_im, basis):
    count = field_re.shape[0]
    side = basis.shape[0]
    stacked = jnp.concatenate([field_re, field_im], axis=0)
    both = jnp.einsum("bjk,kl->bjl", stacked, basis, precision=FAST, preferred_element_type=jnp.float32)
    real = both[:count, :, :side] - both[count:, :, side:]
    imag = both[:count, :, side:] + both[count:, :, :side]
    return (real, imag)


def left_times(basis, field_re, field_im):
    side = basis.shape[1]
    stacked = jnp.concatenate([field_re, field_im], axis=2)
    both = jnp.stack([matmul_fast(basis, one) for one in stacked])
    real = both[:, :side, :side] - both[:, side:, side:]
    imag = both[:, :side, side:] + both[:, side:, :side]
    return (real, imag)


def two_sided(field_re, field_im, bases):
    left, right = bases
    temp_re, temp_im = left_times(left, field_re, field_im)
    return right_times(temp_re, temp_im, right)


def batched_grad(front, back, measured, probe, kernel_re, kernel_im, plain, conjugate):
    first_re, first_im = complex_times(probe[0], probe[1], front[:, 0], front[:, 1])
    spec_re, spec_im = two_sided(first_re, first_im, plain)
    spec_re, spec_im = complex_times(kernel_re, kernel_im, spec_re, spec_im)
    phi_re, phi_im = two_sided(spec_re, spec_im, conjugate)
    exit_re, exit_im = complex_times(phi_re, phi_im, back[:, 0], back[:, 1])
    far_re, far_im = two_sided(exit_re, exit_im, plain)
    misfit = far_re * far_re + far_im * far_im - measured
    return_re, return_im = two_sided(misfit * far_re, misfit * far_im, conjugate)
    second_re, second_im = conj_times(return_re, return_im, phi_re, phi_im)
    wave_re, wave_im = conj_times(return_re, return_im, back[:, 0], back[:, 1])
    wave_re, wave_im = two_sided(wave_re, wave_im, plain)
    wave_re, wave_im = conj_times(wave_re, wave_im, kernel_re, kernel_im)
    wave_re, wave_im = two_sided(wave_re, wave_im, conjugate)
    lead_re, lead_im = conj_times(wave_re, wave_im, probe[0], probe[1])
    return (jnp.stack([lead_re, lead_im], 1), jnp.stack([second_re, second_im], 1))


def passed_along(value, axis, steps):
    count = lax.axis_size(axis)
    first, last = (max(0, -steps), min(count, count - steps))
    return lax.ppermute(value, axis, [(source, source + steps) for source in range(first, last)])


def with_halo(tile_data, half):
    for axis, dim in (("ty", 2), ("tx", 3)):
        length = tile_data.shape[dim]
        before = passed_along(lax.slice_in_dim(tile_data, length - half, length, axis=dim), axis, 1)
        after = passed_along(lax.slice_in_dim(tile_data, 0, half, axis=dim), axis, -1)
        tile_data = jnp.concatenate([before, tile_data, after], axis=dim)
    return tile_data


def fold_halo(canvas, half):
    for axis, dim in (("tx", 3), ("ty", 2)):
        length = canvas.shape[dim]
        size = length - 2 * half
        inner = lax.slice_in_dim(canvas, half, half + size, axis=dim)
        late = passed_along(lax.slice_in_dim(canvas, half + size, length, axis=dim), axis, 1)
        early = passed_along(lax.slice_in_dim(canvas, 0, half, axis=dim), axis, -1)
        widths = [(0, 0)] * canvas.ndim
        widths[dim] = (0, size - half)
        inner = inner + jnp.pad(late, widths)
        widths[dim] = (size - half, 0)
        canvas = inner + jnp.pad(early, widths)
    return canvas


def shards(object_slices, probe, fresnel_phase, intensity, offsets, counts):
    patch = probe.shape[-1]
    half = patch // 2
    tile = object_slices.shape[-1]
    layers = object_slices.shape[0]
    basis_re, basis_im = dft_basis(patch)
    kernel_re = jnp.cos(fresnel_phase)
    kernel_im = jnp.sin(fresnel_phase)
    measured = intensity[0, 0]
    places = offsets[0, 0] + half
    window_shape = (1, 2, patch, patch)
    zero_index = jnp.zeros((), jnp.int32)
    row_here = lax.axis_index("ty")
    col_here = lax.axis_index("tx")
    mine = counts[row_here, col_here]
    plain = (
        jnp.concatenate([basis_re, basis_im], axis=0),
        jnp.concatenate([basis_re, basis_im], axis=1),
    )
    conjugate = (
        jnp.concatenate([basis_re, -basis_im], axis=0),
        jnp.concatenate([basis_re, -basis_im], axis=1),
    )
    slots = measured.shape[0]

    def start_of(slot):
        return (zero_index, zero_index, places[slot, 0], places[slot, 1])

    def windows_of(layer):
        padded = jnp.concatenate([with_halo(object_slices[layer : layer + 1, part : part + 1], half) for part in range(2)], axis=1)
        return jnp.stack([lax.dynamic_slice(padded, start_of(slot), window_shape)[0] for slot in range(slots)])

    span = tile + 2 * half
    block = patch + half
    last_block = (span - block) // half

    def add_at(gradient, slot, term):
        row, col = (places[slot, 0], places[slot, 1])
        block_row = jnp.minimum(row // half, last_block)
        block_col = jnp.minimum(col // half, last_block)
        term = jnp.where(slot < mine, term, jnp.zeros_like(term))
        spread = jnp.pad(term, ((0, 0), (half, half), (half, half)))
        inner = (zero_index, half - (row - block_row * half), half - (col - block_col * half))
        shifted = lax.dynamic_slice(spread, inner, (2, block, block))
        start = (zero_index, block_row * half, block_col * half)
        current = lax.dynamic_slice(gradient, start, shifted.shape)
        return lax.dynamic_update_slice(gradient, current + shifted, start)

    def folded(terms):
        gradient = jnp.zeros((2, span, span), jnp.float32)
        for slot in range(slots):
            gradient = add_at(gradient, slot, terms[slot])
        return jnp.concatenate([fold_halo(gradient[None, part : part + 1], half)[0] for part in range(2)])

    lead, second = batched_grad(windows_of(0), windows_of(1), measured, probe, kernel_re, kernel_im, plain, conjugate)
    core = jnp.stack([folded(lead), folded(second)])
    return object_slices - STEP_SIZE * core


def solution(mesh):
    placed = (
        P(None, None, "ty", "tx"),
        P(),
        P(),
        P("ty", "tx", None, None, None),
        P("ty", "tx", None, None),
        P(),
    )
    return jax.shard_map(
        shards, mesh=mesh, in_specs=placed, out_specs=P(None, None, "ty", "tx"), check_vma=False
    )
```
